32 devices in a mesh: dp: 16 (over z, y, core), head: 2 (over x).
Axes of the slice: x: 2, y: 2, z: 4, core: 2. Of those that a mesh axis runs over, the one named last changes fastest.
Arguments:
- tokens: bfloat16 [2048, 16, 1024], P('head', 'dp'), may hold values from -6 to 6
- lengths: int32 [16], P('dp'), may hold values from 128 to 2048, as said below
- cotangent: bfloat16 [2048, 16, 1024], P('head', 'dp'), may hold values from -6 to 6
- attention_gain: float32 [1024], replicated, may hold values from 0.5 to 1.5
- query_heads: bfloat16 [1024, 96], P(None, 'head'), may hold values from -0.4375 to 0.4375
- key_heads: bfloat16 [1024, 32], P(None, 'head'), may hold values from -0.375 to 0.375
- value_heads: bfloat16 [1024, 32], P(None, 'head'), may hold values from -0.25 to 0.25
- query_basis: bfloat16 [1024, 384], replicated, may hold values from -0.1875 to 0.1875
- key_basis: bfloat16 [1024, 128], replicated, may hold values from -0.1875 to 0.1875
- value_basis: bfloat16 [1024, 128], replicated, may hold values from -0.1875 to 0.1875
- output_weight: bfloat16 [1024, 1024], P('head'), may hold values from -0.75 to 0.75
- feed_gain: float32 [1024], replicated, may hold values from 0.5 to 1.5
- gate_weight: bfloat16 [1024, 2816], P(None, 'head'), may hold values from -0.1875 to 0.1875
- up_weight: bfloat16 [1024, 2816], P(None, 'head'), may hold values from -0.1875 to 0.1875
- down_weight: bfloat16 [2816, 1024], P('head'), may hold values from -0.109375 to 0.109375
Outputs:
- layer_output: bfloat16 [2048, 16, 1024], P('head', 'dp')
- input_grad: float32 [2048, 16, 1024], P('head', 'dp')
- grad_attention_gain: float32 [1024], replicated
- grad_query_heads: float32 [1024, 96], P(None, 'head')
- grad_key_heads: float32 [1024, 32], P(None, 'head')
- grad_value_heads: float32 [1024, 32], P(None, 'head')
- grad_query_basis: float32 [1024, 384], replicated
- grad_key_basis: float32 [1024, 128], replicated
- grad_value_basis: float32 [1024, 128], replicated
- grad_output_weight: float32 [1024, 1024], P('head')
- grad_feed_gain: float32 [1024], replicated
- grad_gate_weight: float32 [1024, 2816], P(None, 'head')
- grad_up_weight: float32 [1024, 2816], P(None, 'head')
- grad_down_weight: float32 [2816, 1024], P('head')
The draws below stay inside these ranges and needn't reach their ends.
Inputs may be any that keep to these rules, and one draw needn't show every extreme that they name: A sequence's first lengths slots hold its tokens; in every draw some sequence fills all 2048 slots.
All inputs are finite; a program needn't handle non-finite values.
Results may differ from the reference program's by a relative error of at most 0.024.
The reference program's roundings to bfloat16 on the way count: a program that leaves them out, or rounds other values in their place, can miss the bound.
Values may be sent and summed in bfloat16 or wider, within the bound.
No kernel may reach another device: no remote copies, remote signals or barrier semaphores. Data moves between devices by JAX's collectives and lax.ppermute only.
A program may use at most 320 MiB of HBM per device.

```python
import jax
import jax.numpy as jnp
from jax import lax

D = 1024
H = 16
DH = 64
RQ = 6
RKV = 2
FF = 2816
SLOTS = 2048
SEQS = 16


def draw_lengths(key, part):
    levels = jax.random.randint(jax.random.fold_in(key, 1), (SEQS,), 0, 4)
    base_length = SLOTS // 16 * jnp.power(jnp.int32(2), levels)
    extra_length = jax.random.randint(jax.random.fold_in(key, 2), (SEQS,), 0, SLOTS) % base_length
    longest = jax.random.randint(jax.random.fold_in(key, 3), (), 0, SEQS)
    drawn = jnp.where(jnp.arange(SEQS) == longest, SLOTS, base_length + extra_length)
    return drawn.astype(jnp.int32)


def block_scale(stream_key, extent, split, smallest, top_value):
    def one(axis_at, parts):
        steps = jax.random.uniform(jax.random.fold_in(jax.random.fold_in(stream_key, 6), axis_at), (parts,), jnp.float32, smallest / len(split), top_value / len(split))
        return jnp.repeat(jnp.exp(steps), extent[axis_at] // parts).reshape((-1,) + (1,) * (len(extent) - axis_at - 1))

    factor_of = one(*split[0])
    for cut in split[1:]:
        factor_of = factor_of * one(*cut)
    return factor_of


def bell_draw(key, dims, scale, bound, split=(), kind=jnp.bfloat16):
    values = jax.random.normal(key, dims, jnp.float32) * scale
    if len(split) > 0:
        values = block_scale(key, dims, split, -0.22, 0.18) * values
    return jnp.clip(values, min=-bound, max=bound).astype(kind)


def setup_inputs(seed: int = 0) -> dict:
    streams_of = jax.random.split(jax.random.key(seed), 16)
    tokens = bell_draw(streams_of[0], (SLOTS, SEQS, D), 1.0, 6.0, ((0, 2), (1, 16)))
    lengths = draw_lengths(jax.random.fold_in(streams_of[15], 71), 0)
    cotangent = bell_draw(streams_of[2], (SLOTS, SEQS, D), 1.0, 6.0, ((0, 2), (1, 16)))
    attention_gain = jnp.clip(1.0 + 0.1 * jax.random.normal(streams_of[3], (D,), jnp.float32), 0.5, 1.5)
    query_heads = bell_draw(streams_of[4], (D, H * RQ), (D // 6) ** -0.5, 0.4375, ((1, 2),))
    key_heads = bell_draw(streams_of[5], (D, H * RKV), (D // 4) ** -0.5, 0.375, ((1, 2),))
    value_heads = bell_draw(streams_of[6], (D, H * RKV), (D // 2) ** -0.5, 0.25, ((1, 2),))
    query_basis = bell_draw(streams_of[7], (D, RQ * DH), D ** -0.5, 0.1875)
    key_basis = bell_draw(streams_of[8], (D, RKV * DH), D ** -0.5, 0.1875)
    value_basis = bell_draw(streams_of[9], (D, RKV * DH), D ** -0.5, 0.1875)
    output_weight = bell_draw(streams_of[10], (H * DH, D), (H * DH // 16) ** -0.5, 0.75, ((0, 2),))
    feed_gain = jnp.clip(1.0 + 0.1 * jax.random.normal(streams_of[11], (D,), jnp.float32), 0.5, 1.5)
    gate_weight = bell_draw(streams_of[12], (D, FF), D ** -0.5, 0.1875, ((1, 2),))
    up_weight = bell_draw(streams_of[13], (D, FF), D ** -0.5, 0.1875, ((1, 2),))
    down_weight = bell_draw(streams_of[14], (FF, D), FF ** -0.5, 0.109375, ((0, 2),))
    return {"tokens": tokens, "lengths": lengths, "cotangent": cotangent, "attention_gain": attention_gain, "query_heads": query_heads, "key_heads": key_heads, "value_heads": value_heads, "query_basis": query_basis, "key_basis": key_basis, "value_basis": value_basis, "output_weight": output_weight, "feed_gain": feed_gain, "gate_weight": gate_weight, "up_weight": up_weight, "down_weight": down_weight}


@jax.custom_vjp
def low(v):
    return lax.optimization_barrier(v.astype(jnp.bfloat16)).astype(jnp.float32)

@jax.custom_vjp
def low_back(v):
    return v

def low_keep(v):
    return (low(v), None)

def low_pass(kept, grad):
    return (grad,)

def back_keep(v):
    return (v, None)

def back_low(kept, grad):
    return (low(grad),)
low.defvjp(low_keep, low_pass)
low_back.defvjp(back_keep, back_low)
norm_eps = 1e-06
masked_score = -1e+30

def product(first_operand, second_operand):
    return jnp.dot(first_operand, second_operand, precision=lax.Precision.HIGHEST, preferred_element_type=jnp.float32)

def contract(pattern, first_operand, second_operand):
    return jnp.einsum(pattern, first_operand, second_operand, precision=lax.Precision.HIGHEST, preferred_element_type=jnp.float32)

def rope_tables(slot_count, head_width):
    half_width = head_width // 2
    inverse = jnp.exp(jnp.arange(half_width, dtype=jnp.float32) * (-2.0 / head_width) * jnp.log(jnp.float32(10000.0)))
    angles = jnp.arange(slot_count, dtype=jnp.float32)[:, None] * inverse[None, :]
    return (jnp.cos(angles), jnp.sin(angles))

def rotate(factor_basis, cosine_table, sine_table):
    half_width = factor_basis.shape[-1] // 2
    lower_half = factor_basis[..., :half_width]
    upper_half = factor_basis[..., half_width:]
    return jnp.concatenate([lower_half * cosine_table - upper_half * sine_table, lower_half * sine_table + upper_half * cosine_table], axis=-1)

def one_head(query_rows, key_rows, value_rows, allowed):
    scores = low_back(product(query_rows, key_rows.T) * DH ** (-0.5))
    scores = jnp.where(allowed, scores, masked_score)
    maxima = lax.optimization_barrier(jnp.max(scores, axis=-1, keepdims=True))
    raised = jnp.exp(scores - maxima)
    probabilities = raised / lax.optimization_barrier(jnp.sum(raised, axis=-1, keepdims=True))
    return product(low(probabilities), value_rows)

def forward(inputs, length, params):
    attention_gain, query_heads, key_heads, value_heads, query_basis, key_basis, value_basis, output_weight, feed_gain, gate_weight, up_weight, down_weight = params
    inv_first = lax.rsqrt(lax.optimization_barrier(jnp.mean(inputs * inputs, axis=-1, keepdims=True)) + norm_eps)
    normed = low(inputs * inv_first * attention_gain)
    head_query = low_back(product(normed, query_heads)).reshape(SLOTS, H, RQ)
    head_key = low_back(product(normed, key_heads)).reshape(SLOTS, H, RKV)
    head_value = low_back(product(normed, value_heads)).reshape(SLOTS, H, RKV)
    basis_query = low_back(product(normed, query_basis)).reshape(SLOTS, RQ, DH)
    basis_key = low_back(product(normed, key_basis)).reshape(SLOTS, RKV, DH)
    basis_value = low_back(product(normed, value_basis)).reshape(SLOTS, RKV, DH)
    cosine_table, sine_table = rope_tables(SLOTS, DH)
    cosine_table = cosine_table[:, None, :]
    sine_table = sine_table[:, None, :]
    turned_query = rotate(basis_query, cosine_table, sine_table)
    turned_key = rotate(basis_key, cosine_table, sine_table)
    queries = low(low_back(contract('shr,srd->shd', head_query, turned_query) / RQ))
    key_all = low(contract('shr,srd->shd', head_key, turned_key) / RKV)
    value_all = low(contract('shr,srd->shd', head_value, basis_value) / RKV)
    positions = jnp.arange(SLOTS, dtype=jnp.int32)
    allowed = (positions[None, :] <= positions[:, None]) & (positions[None, :] < length)
    head_function = jax.checkpoint(lambda triple: one_head(triple[0], triple[1], triple[2], allowed))
    outputs = lax.map(head_function, (queries.transpose(1, 0, 2), key_all.transpose(1, 0, 2), value_all.transpose(1, 0, 2)))
    mixed_heads = low(low_back(outputs.transpose(1, 0, 2).reshape(SLOTS, H * DH)))
    state = inputs + low_back(product(mixed_heads, output_weight))
    inv_second = lax.rsqrt(lax.optimization_barrier(jnp.mean(state * state, axis=-1, keepdims=True)) + norm_eps)
    normed_second = low(state * inv_second * feed_gain)
    gate_in = low_back(product(normed_second, gate_weight))
    up_in = low_back(product(normed_second, up_weight))
    hidden = low(jax.nn.silu(gate_in) * up_in)
    return state + product(hidden, down_weight)

def reference(tokens, lengths, cotangent, attention_gain, query_heads, key_heads, value_heads, query_basis, key_basis, value_basis, output_weight, feed_gain, gate_weight, up_weight, down_weight):
    params = tuple((weight.astype(jnp.float32) for weight in (attention_gain, query_heads, key_heads, value_heads, query_basis, key_basis, value_basis, output_weight, feed_gain, gate_weight, up_weight, down_weight)))
    inputs_all = tokens.astype(jnp.float32).transpose(1, 0, 2)
    outgrad_all = cotangent.astype(jnp.float32).transpose(1, 0, 2)

    def per_sequence(totals, sequence_item):
        inputs, outgrad, length = sequence_item

        def apply_layer(inputs_one, *weights):
            return forward(inputs_one, length, weights)
        result, pullback = jax.vjp(apply_layer, inputs, *params)
        all_grads = pullback(outgrad)
        summed = tuple((total + grad_one for total, grad_one in zip(totals, all_grads[1:])))
        return (summed, (result, all_grads[0]))
    zero_grads = tuple((jnp.zeros_like(weight) for weight in params))
    totals, (results, input_grads) = lax.scan(per_sequence, zero_grads, (inputs_all, outgrad_all, lengths))
    layer_output = results.transpose(1, 0, 2).astype(jnp.bfloat16)
    input_grad = input_grads.transpose(1, 0, 2)
    return (layer_output, input_grad, totals[0], totals[1], totals[2], totals[3], totals[4], totals[5], totals[6], totals[7], totals[8], totals[9], totals[10], totals[11])
```

```python
import jax
import jax.numpy as jnp
from jax import lax
from jax.sharding import PartitionSpec as P
from jax.experimental import pallas as pl
from jax.experimental.pallas import tpu as pltpu
import functools

MASKED = -1e30


def _mask(s, row0, col0, length):
    rows = row0 + lax.broadcasted_iota(jnp.int32, s.shape, 0)
    cols = col0 + lax.broadcasted_iota(jnp.int32, s.shape, 1)
    allowed = (cols <= rows) & (cols < length)
    return jnp.where(allowed, s, MASKED)


def _fwd_kernel(len_ref, q_ref, k_ref, v_ref, o_ref, of_ref, m_ref, il_ref, s_scr, *, tq, tk, scale):
    qb = pl.program_id(1)
    length = len_ref[0]
    n_kb = jnp.minimum((qb * tq + tq + tk - 1) // tk, (length + tk - 1) // tk)
    q = q_ref[0]

    def pass_one(kb, carry):
        m, l = carry
        k = k_ref[0, pl.ds(pl.multiple_of(kb * tk, tk), tk), :]
        s = lax.dot_general(q, k, (((1,), (1,)), ((), ())), preferred_element_type=jnp.float32) * scale
        s = _mask(s, qb * tq, kb * tk, length)
        s_scr[kb] = s
        m_new = jnp.maximum(m, jnp.max(s, axis=1, keepdims=True))
        l = l * jnp.exp(m - m_new) + jnp.sum(jnp.exp(s - m_new), axis=1, keepdims=True)
        return m_new, l

    m0 = jnp.full((tq, 1), -jnp.inf, jnp.float32)
    l0 = jnp.zeros((tq, 1), jnp.float32)
    m, l = lax.fori_loop(0, n_kb, pass_one, (m0, l0))
    inv_l = 1.0 / l

    def pass_two(kb, carry):
        acc, low = carry
        p = jnp.exp(s_scr[kb] - m) * inv_l
        p_high = p.astype(jnp.bfloat16)
        p_low = (p - p_high.astype(jnp.float32)).astype(jnp.bfloat16)
        v = v_ref[0, pl.ds(pl.multiple_of(kb * tk, tk), tk), :]
        acc = acc + jnp.dot(p_high, v, preferred_element_type=jnp.float32)
        low = low + jnp.dot(p_low, v, preferred_element_type=jnp.float32)
        return acc, low

    zero = jnp.zeros(o_ref.shape[1:], jnp.float32)
    acc, low = lax.fori_loop(0, n_kb, pass_two, (zero, zero))
    o_ref[0] = acc.astype(o_ref.dtype)
    of_ref[0] = acc + low
    m_ref[0] = m
    il_ref[0] = inv_l


def attention_fwd(q, k, v, length, *, tq=256, tk=256):
    heads, slots, width = q.shape
    nq = slots // tq
    kernel = functools.partial(_fwd_kernel, tq=tq, tk=tk, scale=width ** (-0.5))
    return pl.pallas_call(
        kernel,
        out_shape=(
            jax.ShapeDtypeStruct((heads, slots, width), jnp.bfloat16),
            jax.ShapeDtypeStruct((heads, slots, width), jnp.float32),
            jax.ShapeDtypeStruct((heads, slots, 1), jnp.float32),
            jax.ShapeDtypeStruct((heads, slots, 1), jnp.float32),
        ),
        grid_spec=pltpu.PrefetchScalarGridSpec(
            num_scalar_prefetch=1,
            grid=(heads, nq),
            in_specs=[
                pl.BlockSpec((1, tq, width), lambda h, i, n: (h, i, 0)),
                pl.BlockSpec((1, slots, width), lambda h, i, n: (h, 0, 0)),
                pl.BlockSpec((1, slots, width), lambda h, i, n: (h, 0, 0)),
            ],
            out_specs=[
                pl.BlockSpec((1, tq, width), lambda h, i, n: (h, i, 0)),
                pl.BlockSpec((1, tq, width), lambda h, i, n: (h, i, 0)),
                pl.BlockSpec((1, tq, 1), lambda h, i, n: (h, i, 0)),
                pl.BlockSpec((1, tq, 1), lambda h, i, n: (h, i, 0)),
            ],
            scratch_shapes=[pltpu.VMEM((slots // tk, tq, tk), jnp.float32)],
        ),
        compiler_params=pltpu.CompilerParams(dimension_semantics=("arbitrary", "arbitrary")),
        cost_estimate=pl.CostEstimate(
            flops=2 * heads * slots * slots * width, transcendentals=heads * slots * slots,
            bytes_accessed=4 * heads * slots * width * 2),
    )(length.reshape(1), q, k, v)


def _bwd_kernel(len_ref, q_ref, k_ref, v_ref, g_ref, m_ref, il_ref, d_ref,
                dq_ref, dk_ref, dv_ref, dq_scr, *, tq, tk, scale):
    length = len_ref[0]
    slots = q_ref.shape[1]
    nq = slots // tq
    n_kb = (length + tk - 1) // tk
    dq_scr[...] = jnp.zeros(dq_scr.shape, jnp.float32)
    dk_ref[...] = jnp.zeros(dk_ref.shape, jnp.float32)
    dv_ref[...] = jnp.zeros(dv_ref.shape, jnp.float32)

    def key_block(kb, _):
        kstart = pl.multiple_of(kb * tk, tk)
        k = k_ref[0, pl.ds(kstart, tk), :]
        v = v_ref[0, pl.ds(kstart, tk), :]
        first_qb = (kb * tk) // tq

        def query_block(qb, carry):
            dk_acc, dv_acc = carry
            qstart = pl.multiple_of(qb * tq, tq)
            q = q_ref[0, pl.ds(qstart, tq), :]
            g = g_ref[0, pl.ds(qstart, tq), :]
            s = lax.dot_general(q, k, (((1,), (1,)), ((), ())), preferred_element_type=jnp.float32) * scale
            s = _mask(s, qb * tq, kb * tk, length)
            p = jnp.exp(s - m_ref[0, pl.ds(qstart, tq), :]) * il_ref[0, pl.ds(qstart, tq), :]
            dp = lax.dot_general(g, v, (((1,), (1,)), ((), ())), preferred_element_type=jnp.float32)
            ds = (p * (dp - d_ref[0, pl.ds(qstart, tq), :])).astype(jnp.bfloat16)
            dv_acc = dv_acc + lax.dot_general(p.astype(jnp.bfloat16), g, (((0,), (0,)), ((), ())),
                                              preferred_element_type=jnp.float32)
            dk_acc = dk_acc + lax.dot_general(ds, q, (((0,), (0,)), ((), ())),
                                              preferred_element_type=jnp.float32)
            dq_scr[pl.ds(qstart, tq), :] += jnp.dot(ds, k, preferred_element_type=jnp.float32)
            return dk_acc, dv_acc

        zero = jnp.zeros((tk, k_ref.shape[2]), jnp.float32)
        dk_acc, dv_acc = lax.fori_loop(first_qb, nq, query_block, (zero, zero))
        dk_ref[0, pl.ds(kstart, tk), :] = dk_acc * scale
        dv_ref[0, pl.ds(kstart, tk), :] = dv_acc
        return 0

    lax.fori_loop(0, n_kb, key_block, 0)
    dq_ref[0] = (dq_scr[...] * scale).astype(dq_ref.dtype)


def attention_bwd(q, k, v, g, m, inv_l, centre, length, *, tq=256, tk=256):
    heads, slots, width = q.shape
    kernel = functools.partial(_bwd_kernel, tq=tq, tk=tk, scale=width ** (-0.5))
    full = pl.BlockSpec((1, slots, width), lambda h, n: (h, 0, 0))
    col = pl.BlockSpec((1, slots, 1), lambda h, n: (h, 0, 0))
    return pl.pallas_call(
        kernel,
        out_shape=(
            jax.ShapeDtypeStruct((heads, slots, width), jnp.bfloat16),
            jax.ShapeDtypeStruct((heads, slots, width), jnp.float32),
            jax.ShapeDtypeStruct((heads, slots, width), jnp.float32),
        ),
        grid_spec=pltpu.PrefetchScalarGridSpec(
            num_scalar_prefetch=1,
            grid=(heads,),
            in_specs=[full, full, full, full, col, col, col],
            out_specs=[full, full, full],
            scratch_shapes=[pltpu.VMEM((slots, width), jnp.float32)],
        ),
        compiler_params=pltpu.CompilerParams(dimension_semantics=("arbitrary",)),
        cost_estimate=pl.CostEstimate(
            flops=5 * heads * slots * slots * width, transcendentals=heads * slots * slots // 2,
            bytes_accessed=heads * slots * width * 16),
    )(length.reshape(1), q, k, v, g, m, inv_l, centre)


RQ = 6
RKV = 2


norm_eps = 1e-06
masked_score = -1e30


def rope_tables(slot_count, head_width):
    half_width = head_width // 2
    inverse = jnp.exp(
        jnp.arange(half_width, dtype=jnp.float32)
        * (-2.0 / head_width)
        * jnp.log(jnp.float32(10000.0))
    )
    angles = jnp.arange(slot_count, dtype=jnp.float32)[:, None] * inverse[None, :]
    return (jnp.cos(angles), jnp.sin(angles))


def rotate(factor_basis, cosine_table, sine_table):
    half_width = factor_basis.shape[-1] // 2
    lower_half = factor_basis[..., :half_width]
    upper_half = factor_basis[..., half_width:]
    return jnp.concatenate(
        [
            lower_half * cosine_table - upper_half * sine_table,
            lower_half * sine_table + upper_half * cosine_table,
        ],
        axis=-1,
    )


def unrotate(turned_grad, cosine_table, sine_table):
    half_width = turned_grad.shape[-1] // 2
    lower_half = turned_grad[..., :half_width]
    upper_half = turned_grad[..., half_width:]
    return jnp.concatenate(
        [
            lower_half * cosine_table + upper_half * sine_table,
            upper_half * cosine_table - lower_half * sine_table,
        ],
        axis=-1,
    )


def matmul(first_operand, second_operand):
    return jnp.dot(first_operand, second_operand, preferred_element_type=jnp.float32)


def mix_rank(head_part, turned_part):
    total = head_part[..., 0][..., None] * turned_part[:, :, 0][:, :, None, :]
    for rank_index in range(1, head_part.shape[-1]):
        total = (
            total
            + head_part[..., rank_index][..., None] * turned_part[:, :, rank_index][:, :, None, :]
        )
    return total


def combine(head_part, turned_part, rank):
    return (mix_rank(head_part, turned_part) / rank).astype(jnp.bfloat16)


def factor_grad(grad_rows, turned_part, rank):
    pieces = [
        jnp.sum(grad_rows * turned_part[:, :, rank_index][:, :, None, :], axis=-1)
        for rank_index in range(turned_part.shape[2])
    ]
    return jnp.stack(pieces, axis=-1) / rank


def basis_grad_of(grad_rows, head_part, rank):
    pieces = [
        jnp.sum(grad_rows * head_part[..., rank_index][..., None], axis=2)
        for rank_index in range(head_part.shape[-1])
    ]
    return jnp.stack(pieces, axis=2) / rank


def per_device(
    tokens,
    lengths,
    cotangent,
    attention_gain,
    query_heads,
    key_heads,
    value_heads,
    query_basis,
    key_basis,
    value_basis,
    output_weight,
    feed_gain,
    gate_weight,
    up_weight,
    down_weight,
):
    head_group = lax.axis_size("head")
    part_slots, sequences, model_width = tokens.shape
    all_slots = part_slots * head_group
    local_rows = part_slots * sequences
    full_rows = all_slots * sequences
    head_width = query_basis.shape[1] // RQ
    score_scale = head_width ** (-0.5)
    cosine_all, sine_all = rope_tables(all_slots, head_width)
    basis_cat = jnp.concatenate([query_basis, key_basis, value_basis], axis=1)
    basis_query_cols = RQ * head_width
    basis_pair_cols = RKV * head_width
    positions = jnp.arange(all_slots, dtype=jnp.int32)

    def row_slice(source, row_start, row_count):
        return lax.dynamic_slice_in_dim(source, row_start, row_count, 0)

    def split_heads(head_proj, slot_count, heads_count):
        query_cols = heads_count * RQ
        pair_cols = heads_count * RKV
        head_query = head_proj[:, :query_cols].reshape(slot_count, sequences, heads_count, RQ)
        head_key = head_proj[:, query_cols : query_cols + pair_cols].reshape(
            slot_count, sequences, heads_count, RKV
        )
        head_value = head_proj[:, query_cols + pair_cols :].reshape(
            slot_count, sequences, heads_count, RKV
        )
        return (head_query, head_key, head_value)

    def split_basis(basis_proj, slot_count, cosine_table, sine_table):
        turned_query = rotate(
            basis_proj[:, :basis_query_cols].reshape(slot_count, sequences, RQ, head_width),
            cosine_table,
            sine_table,
        )
        turned_key = rotate(
            basis_proj[:, basis_query_cols : basis_query_cols + basis_pair_cols].reshape(
                slot_count, sequences, RKV, head_width
            ),
            cosine_table,
            sine_table,
        )
        basis_value = basis_proj[:, basis_query_cols + basis_pair_cols :].reshape(
            slot_count, sequences, RKV, head_width
        )
        return (turned_query, turned_key, basis_value)

    inputs = tokens.reshape(local_rows, model_width).astype(jnp.float32)
    inv_first = lax.rsqrt(jnp.mean(inputs * inputs, axis=-1, keepdims=True) + norm_eps)
    normed = (inputs * inv_first * attention_gain).astype(jnp.bfloat16)
    heads_here = query_heads.shape[1] // RQ
    head_cat = jnp.concatenate([query_heads, key_heads, value_heads], axis=1)
    query_cols = heads_here * RQ
    pair_cols = heads_here * RKV
    cosine_full = cosine_all[:, None, None, :]
    sine_full = sine_all[:, None, None, :]
    normed_full = lax.all_gather(
        normed.reshape(part_slots, sequences, model_width), "head", axis=0, tiled=True
    ).reshape(full_rows, model_width)

    def full_factors():
        head_proj = matmul(normed_full, head_cat)
        basis_proj = matmul(normed_full, basis_cat)
        head_query, head_key, head_value = split_heads(head_proj, all_slots, heads_here)
        turned_query, turned_key, basis_value = split_basis(
            basis_proj, all_slots, cosine_full, sine_full
        )
        return (head_query, head_key, head_value, turned_query, turned_key, basis_value)

    head_query, head_key, head_value, turned_query, turned_key, basis_value = full_factors()
    query_all = combine(head_query, turned_query, RQ)
    key_all = combine(head_key, turned_key, RKV)
    value_all = combine(head_value, basis_value, RKV)
    length = lengths[0]
    query_heads_major = query_all[:, 0].transpose(1, 0, 2)
    key_heads_major = key_all[:, 0].transpose(1, 0, 2)
    value_heads_major = value_all[:, 0].transpose(1, 0, 2)
    out_heads, out_full, row_max, row_inv = attention_fwd(
        query_heads_major, key_heads_major, value_heads_major, length
    )
    mixed_heads = out_heads.transpose(1, 0, 2).reshape(full_rows, heads_here * head_width)
    attention_out = lax.psum_scatter(
        matmul(
            row_slice(mixed_heads, jnp.int32(0), local_rows * lax.axis_size("head")), output_weight
        ).astype(jnp.bfloat16),
        "head",
        scatter_dimension=0,
        tiled=True,
    ).astype(jnp.float32)
    state = inputs + attention_out
    inv_second = lax.rsqrt(jnp.mean(state * state, axis=-1, keepdims=True) + norm_eps)
    normed_second = (state * inv_second * feed_gain).astype(jnp.bfloat16)
    out_grad = cotangent.reshape(local_rows, model_width)
    feed_rows = lax.all_gather(
        normed_second.reshape(part_slots, sequences, model_width), "head", axis=0, tiled=True
    ).reshape(full_rows, model_width)
    gate_in = matmul(feed_rows, gate_weight)
    up_in = matmul(feed_rows, up_weight)
    sigmoid_gate = jax.nn.sigmoid(gate_in)
    hidden_low = (gate_in * sigmoid_gate * up_in).astype(jnp.bfloat16)
    feed_out = lax.psum_scatter(
        matmul(
            row_slice(hidden_low, jnp.int32(0), local_rows * lax.axis_size("head")), down_weight
        ).astype(jnp.bfloat16),
        "head",
        scatter_dimension=0,
        tiled=True,
    ).astype(jnp.float32)
    layer_output = (
        (state + feed_out).astype(jnp.bfloat16).reshape(part_slots, sequences, model_width)
    )
    out_grad_full = lax.all_gather(cotangent, "head", axis=0, tiled=True).reshape(
        full_rows, model_width
    )
    hidden_grad = matmul(out_grad_full, down_weight.T)
    grad_down = matmul(hidden_low.T, out_grad_full)
    gate_grad = (
        hidden_grad * up_in * sigmoid_gate * (1.0 + gate_in * (1.0 - sigmoid_gate))
    ).astype(jnp.bfloat16)
    up_grad = (hidden_grad * gate_in * sigmoid_gate).astype(jnp.bfloat16)
    grad_gate = matmul(feed_rows.T, gate_grad)
    grad_up = matmul(feed_rows.T, up_grad)
    row_start = jnp.int32(0)
    normed_second_grad = lax.psum_scatter(
        (
            matmul(
                row_slice(gate_grad, row_start, local_rows * lax.axis_size("head")), gate_weight.T
            )
            + matmul(row_slice(up_grad, row_start, local_rows * lax.axis_size("head")), up_weight.T)
        ).astype(jnp.bfloat16),
        "head",
        scatter_dimension=0,
        tiled=True,
    ).astype(jnp.float32)
    scaled_second = feed_gain * normed_second_grad
    gain_second_grad = jnp.sum(normed_second_grad * state * inv_second, axis=0)
    state_grad = (
        out_grad.astype(jnp.float32)
        + inv_second * scaled_second
        - state * inv_second**3 * jnp.mean(scaled_second * state, axis=-1, keepdims=True)
    )
    attention_grad = state_grad.astype(jnp.bfloat16)
    attention_grad_full = lax.all_gather(
        attention_grad.reshape(part_slots, sequences, model_width), "head", axis=0, tiled=True
    ).reshape(full_rows, model_width)
    grad_output = matmul(mixed_heads.T, attention_grad_full)
    heads_grad = (
        matmul(attention_grad_full, output_weight.T)
        .astype(jnp.bfloat16)
        .reshape(all_slots, sequences, heads_here, head_width)
    )
    grad_heads_major = heads_grad[:, 0].transpose(1, 0, 2)
    centre = jnp.sum(grad_heads_major.astype(jnp.float32) * out_full, axis=-1, keepdims=True)
    query_grad, key_grad, value_grad = attention_bwd(
        query_heads_major, key_heads_major, value_heads_major, grad_heads_major,
        row_max, row_inv, centre, length,
    )
    query_grads = [query_grad.transpose(1, 0, 2)]
    key_grads = [key_grad.transpose(1, 0, 2)]
    value_grads = [value_grad.transpose(1, 0, 2)]
    query_grad_all = jnp.stack(query_grads, axis=1).astype(jnp.float32)
    key_grad_all = jnp.stack(key_grads, axis=1)
    value_grad_all = jnp.stack(value_grads, axis=1)
    head_query_grad = factor_grad(query_grad_all, turned_query, RQ).astype(jnp.bfloat16)
    head_key_grad = factor_grad(key_grad_all, turned_key, RKV).astype(jnp.bfloat16)
    head_value_grad = factor_grad(value_grad_all, basis_value, RKV).astype(jnp.bfloat16)
    turned_query_grad = basis_grad_of(query_grad_all, head_query, RQ)
    turned_key_grad = basis_grad_of(key_grad_all, head_key, RKV)
    basis_value_grad = basis_grad_of(value_grad_all, head_value, RKV)
    head_grad_cat = jnp.concatenate(
        [
            head_query_grad.reshape(full_rows, query_cols),
            head_key_grad.reshape(full_rows, pair_cols),
            head_value_grad.reshape(full_rows, pair_cols),
        ],
        axis=1,
    )
    basis_grad_cat = jnp.concatenate(
        [
            unrotate(turned_query_grad, cosine_full, sine_full).reshape(
                full_rows, basis_query_cols
            ),
            unrotate(turned_key_grad, cosine_full, sine_full).reshape(full_rows, basis_pair_cols),
            basis_value_grad.reshape(full_rows, basis_pair_cols),
        ],
        axis=1,
    )
    grad_heads = matmul(normed_full.T, head_grad_cat)
    grad_query_part = grad_heads[:, :query_cols]
    grad_key_part = grad_heads[:, query_cols : query_cols + pair_cols]
    grad_value_part = grad_heads[:, query_cols + pair_cols :]
    row_start = jnp.int32(0)
    head_part = row_slice(head_grad_cat, row_start, local_rows * lax.axis_size("head"))
    basis_part = row_slice(basis_grad_cat, row_start, local_rows * lax.axis_size("head"))
    back_slice = lax.psum_scatter(
        jnp.concatenate([matmul(head_part, head_cat.T), basis_part], axis=1).astype(jnp.bfloat16),
        "head",
        scatter_dimension=0,
        tiled=True,
    ).astype(jnp.float32)
    basis_grad_low = back_slice[:, model_width:].astype(jnp.bfloat16)
    normed_grad = back_slice[:, :model_width] + matmul(basis_grad_low, basis_cat.T)
    grad_basis = matmul(normed.T, basis_grad_low)
    scaled_first = attention_gain * normed_grad
    gain_first_grad = jnp.sum(normed_grad * inputs * inv_first, axis=0)
    input_grad = (
        state_grad
        + inv_first * scaled_first
        - inputs * inv_first**3 * jnp.mean(scaled_first * inputs, axis=-1, keepdims=True)
    )
    summed_heads = (
        lax.psum(grad_query_part.astype(jnp.bfloat16), "dp").astype(jnp.float32),
        lax.psum(grad_key_part.astype(jnp.bfloat16), "dp").astype(jnp.float32),
        lax.psum(grad_value_part.astype(jnp.bfloat16), "dp").astype(jnp.float32),
        lax.psum(grad_output.astype(jnp.bfloat16), "dp").astype(jnp.float32),
        lax.psum(grad_gate.astype(jnp.bfloat16), "dp").astype(jnp.float32),
        lax.psum(grad_up.astype(jnp.bfloat16), "dp").astype(jnp.float32),
        lax.psum(grad_down.astype(jnp.bfloat16), "dp").astype(jnp.float32),
    )
    summed_shared = lax.psum(
        (
            grad_basis[:, :basis_query_cols],
            grad_basis[:, basis_query_cols : basis_query_cols + basis_pair_cols],
            grad_basis[:, basis_query_cols + basis_pair_cols :],
            gain_first_grad,
            gain_second_grad,
        ),
        ("dp", "head"),
    )
    return (
        layer_output,
        input_grad.reshape(part_slots, sequences, model_width),
        summed_shared[3],
        summed_heads[0],
        summed_heads[1],
        summed_heads[2],
        summed_shared[0],
        summed_shared[1],
        summed_shared[2],
        summed_heads[3],
        summed_shared[4],
        summed_heads[4],
        summed_heads[5],
        summed_heads[6],
    )


def solution(mesh):
    in_specs = (
        P("head", "dp", None),
        P("dp"),
        P("head", "dp", None),
        P(),
        P(None, "head"),
        P(None, "head"),
        P(None, "head"),
        P(),
        P(),
        P(),
        P("head", None),
        P(),
        P(None, "head"),
        P(None, "head"),
        P("head", None),
    )
    out_specs = (
        P("head", "dp", None),
        P("head", "dp", None),
        P(),
        P(None, "head"),
        P(None, "head"),
        P(None, "head"),
        P(),
        P(),
        P(),
        P("head", None),
        P(),
        P(None, "head"),
        P(None, "head"),
        P("head", None),
    )
    return jax.shard_map(
        per_device, mesh=mesh, in_specs=in_specs, out_specs=out_specs, check_vma=False
    )
```
